512 devices in a mesh: space: 64 (over z, x, core), snap: 8 (over y).
Axes of the slice: x: 4, y: 8, z: 8, core: 2. Of those that a mesh axis runs over, the one named last changes fastest.
Arguments:
- snapshots: bfloat16 [262144, 2048], P('space', 'snap'), may hold values from -6 to 6
- basis: bfloat16 [262144, 64], P('space'), may hold values from -0.01171875 to 0.01171875
Outputs:
- normal: float32 [2144, 2144], P('snap')
- rhs: float32 [2144, 64], P('snap')
The draws below stay inside these ranges and needn't reach their ends.
All inputs are finite; a program needn't handle non-finite values.
Results may differ from the reference program's by a relative error of at most 0.0034.
Values sent between devices are 32-bit elements; how exact they have to be, the bound alone decides.
No kernel may reach another device: no remote copies, remote signals or barrier semaphores. Data moves between devices by JAX's collectives and lax.ppermute only.
A program may use at most 64 MiB of HBM per device.

```python
import jax
import jax.numpy as jnp
import numpy as np

R = 64
NSPACE = 262144
NT = 2048


def shard_levels(stream_key, extent, cuts, smallest, high):
    loudness, own = 1.0, jax.random.fold_in(stream_key, 6)
    for dim, blocks in cuts:
        draws = jnp.exp(jax.random.uniform(jax.random.fold_in(own, dim), (blocks,), jnp.float32, smallest / len(cuts), high / len(cuts)))
        loudness = loudness * jnp.repeat(draws, extent[dim] // blocks).reshape([-1 if axis == dim else 1 for axis in range(len(extent))])
    return loudness


def normal_values(rng, dims, deviation, limit, cuts=(), kind=jnp.bfloat16):
    result = deviation * jax.random.normal(rng, dims, jnp.float32)
    if cuts:
        result = result * shard_levels(rng, dims, cuts, -0.22, 0.18)
    return jnp.clip(result, -limit, limit).astype(kind)


def setup_inputs(seed: int = 0) -> dict:
    keys = jax.random.split(jax.random.key(seed), 3)
    snapshots = normal_values(keys[0], (NSPACE, NT), 1.0, 6.0, ((0, 64), (1, 8)))
    basis = normal_values(keys[1], (NSPACE, R), NSPACE ** -0.5, 0.01171875, ((0, 64),))
    return dict(snapshots=snapshots, basis=basis)


def make_features(states):
    upper_rows, upper_cols = np.triu_indices(R)
    quad = states[upper_rows, :] * states[upper_cols, :]
    return jnp.concatenate([states, quad], axis=0).T.astype(jnp.bfloat16)


def reference(snapshots, basis):
    states = jnp.dot(basis.T, snapshots, preferred_element_type=jnp.float32)
    targets = (jnp.roll(states, -1, axis=1) - states).T.astype(jnp.bfloat16)
    features = make_features(states)
    normal = jnp.dot(features.T, features, preferred_element_type=jnp.float32) / NT
    rhs = jnp.dot(features.T, targets, preferred_element_type=jnp.float32) / NT
    return normal, rhs
```

```python
import jax
import jax.numpy as jnp
import numpy as np
from jax import lax
from jax.experimental import pallas as pl
from jax.experimental.pallas import tpu as pltpu
from jax.sharding import PartitionSpec as P


def swapped(block, axis, distance):
    count = lax.axis_size(axis)
    return lax.ppermute(block, axis, [(i, i ^ distance) for i in range(count)])


def butterfly_sum(block, axis):
    distance = 1
    while distance < lax.axis_size(axis):
        block = block + swapped(block, axis, distance)
        distance *= 2
    return block


def butterfly_gather(block, axis):
    index = lax.axis_index(axis)
    distance = 1
    while distance < lax.axis_size(axis):
        other = swapped(block, axis, distance)
        low = (index // distance) % 2 == 0
        block = jnp.where(
            low,
            jnp.concatenate([block, other], axis=1),
            jnp.concatenate([other, block], axis=1),
        )
        distance *= 2
    return block


def feature_kernel(states_ref, out_ref, rows_ref):
    rank = states_ref.shape[0]
    rows_ref[0:rank, :] = states_ref[...]
    offset = rank
    for a in range(rank):
        count = rank - a
        rows_ref[offset : offset + count, :] = states_ref[a : a + 1, :] * states_ref[a:rank, :]
        offset += count
    out_ref[...] = rows_ref[...].astype(out_ref.dtype)


def features_t(states, lanes=256):
    rank, snaps = states.shape
    width = rank + rank * (rank + 1) // 2
    return pl.pallas_call(
        feature_kernel,
        grid=(snaps // lanes,),
        in_specs=[pl.BlockSpec((rank, lanes), lambda j: (0, j))],
        out_specs=pl.BlockSpec((width, lanes), lambda j: (0, j)),
        out_shape=jax.ShapeDtypeStruct((width, snaps), jnp.bfloat16),
        scratch_shapes=[pltpu.VMEM((width, lanes), jnp.float32)],
        cost_estimate=pl.CostEstimate(
            flops=width * snaps, transcendentals=0, bytes_accessed=rank * snaps * 4 + width * snaps * 2
        ),
    )(states)


def per_device(snapshots, basis):
    partial_value = lax.dot_general(
        basis, snapshots, (((0,), (0,)), ((), ())), preferred_element_type=jnp.float32
    )
    reduced = butterfly_sum(partial_value, "space")
    states = butterfly_gather(reduced, "snap")
    total_snaps = states.shape[1]
    feats = features_t(states)
    targets = (jnp.roll(states, -1, axis=1) - states).astype(jnp.bfloat16)
    width = feats.shape[0]
    block_rows = width // lax.axis_size("snap")
    chosen = lax.dynamic_slice_in_dim(feats, lax.axis_index("snap") * block_rows, block_rows, 0)
    dims = (((1,), (1,)), ((), ()))
    normal = lax.dot_general(chosen, feats, dims, preferred_element_type=jnp.float32) / total_snaps
    rhs = lax.dot_general(chosen, targets, dims, preferred_element_type=jnp.float32) / total_snaps
    return (normal, rhs)


def solution(mesh):
    return jax.shard_map(
        per_device,
        mesh=mesh,
        in_specs=(P("space", "snap"), P("space", None)),
        out_specs=(P("snap", None), P("snap", None)),
        check_vma=False,
    )
```

```python
import jax
import jax.numpy as jnp
import numpy as np
from jax import lax
from jax.experimental import pallas as pl
from jax.experimental.pallas import tpu as pltpu
from jax.sharding import PartitionSpec as P


def swapped(block, axis, distance):
    count = lax.axis_size(axis)
    return lax.ppermute(block, axis, [(i, i ^ distance) for i in range(count)])


def butterfly_sum(block, axis):
    distance = 1
    while distance < lax.axis_size(axis):
        block = block + swapped(block, axis, distance)
        distance *= 2
    return block


def butterfly_gather(block, axis):
    index = lax.axis_index(axis)
    distance = 1
    while distance < lax.axis_size(axis):
        other = swapped(block, axis, distance)
        low = (index // distance) % 2 == 0
        block = jnp.where(
            low,
            jnp.concatenate([block, other], axis=1),
            jnp.concatenate([other, block], axis=1),
        )
        distance *= 2
    return block


def feature_kernel(states_ref, out_ref, rows_ref):
    rank = states_ref.shape[0]
    rows_ref[0:rank, :] = states_ref[...]
    offset = rank
    for a in range(rank):
        count = rank - a
        rows_ref[offset : offset + count, :] = states_ref[a : a + 1, :] * states_ref[a:rank, :]
        offset += count
    out_ref[...] = rows_ref[...].astype(out_ref.dtype)


def features_t(states, lanes=256):
    rank, snaps = states.shape
    width = rank + rank * (rank + 1) // 2
    return pl.pallas_call(
        feature_kernel,
        grid=(snaps // lanes,),
        in_specs=[pl.BlockSpec((rank, lanes), lambda j: (0, j))],
        out_specs=pl.BlockSpec((width, lanes), lambda j: (0, j)),
        out_shape=jax.ShapeDtypeStruct((width, snaps), jnp.bfloat16),
        scratch_shapes=[pltpu.VMEM((width, lanes), jnp.float32)],
        cost_estimate=pl.CostEstimate(
            flops=width * snaps, transcendentals=0, bytes_accessed=rank * snaps * 4 + width * snaps * 2
        ),
    )(states)


def per_device(snapshots, basis):
    partial_value = lax.dot_general(
        basis, snapshots, (((0,), (0,)), ((), ())), preferred_element_type=jnp.float32
    )
    rank, columns = partial_value.shape
    groups = lax.axis_size("space")
    snaps = lax.axis_size("snap")
    chunks = partial_value.reshape(rank, groups, columns // groups)
    received = lax.all_to_all(chunks, "space", 1, 1, tiled=True)
    owned = jnp.sum(received, axis=1)
    spread = jnp.broadcast_to(owned[:, None, :], (rank, groups * snaps, owned.shape[1]))
    everyone = lax.all_to_all(spread, ("space", "snap"), 1, 1, tiled=True)
    states = (
        everyone.reshape(rank, groups, snaps, -1).transpose(0, 2, 1, 3).reshape(rank, columns * snaps)
    )
    total_snaps = states.shape[1]
    feats = features_t(states)
    targets = (jnp.roll(states, -1, axis=1) - states).astype(jnp.bfloat16)
    width = feats.shape[0]
    block_rows = width // snaps
    chosen = lax.dynamic_slice_in_dim(feats, lax.axis_index("snap") * block_rows, block_rows, 0)
    dims = (((1,), (1,)), ((), ()))
    normal = lax.dot_general(chosen, feats, dims, preferred_element_type=jnp.float32) / total_snaps
    rhs = lax.dot_general(chosen, targets, dims, preferred_element_type=jnp.float32) / total_snaps
    return (normal, rhs)


def solution(mesh):
    return jax.shard_map(
        per_device,
        mesh=mesh,
        in_specs=(P("space", "snap"), P("space", None)),
        out_specs=(P("snap", None), P("snap", None)),
        check_vma=False,
    )
```

```python
import jax
import jax.numpy as jnp
import numpy as np
from jax import lax
from jax.experimental import pallas as pl
from jax.experimental.pallas import tpu as pltpu
from jax.sharding import PartitionSpec as P


def swapped(block, axis, distance):
    count = lax.axis_size(axis)
    return lax.ppermute(block, axis, [(i, i ^ distance) for i in range(count)])


def butterfly_sum(block, axis):
    distance = 1
    while distance < lax.axis_size(axis):
        block = block + swapped(block, axis, distance)
        distance *= 2
    return block


def butterfly_gather(block, axis):
    index = lax.axis_index(axis)
    distance = 1
    while distance < lax.axis_size(axis):
        other = swapped(block, axis, distance)
        low = (index // distance) % 2 == 0
        block = jnp.where(
            low,
            jnp.concatenate([block, other], axis=1),
            jnp.concatenate([other, block], axis=1),
        )
        distance *= 2
    return block


def feature_kernel(states_ref, out_ref, rows_ref):
    rank = states_ref.shape[0]
    rows_ref[0:rank, :] = states_ref[...]
    offset = rank
    for a in range(rank):
        count = rank - a
        rows_ref[offset : offset + count, :] = states_ref[a : a + 1, :] * states_ref[a:rank, :]
        offset += count
    out_ref[...] = rows_ref[...].astype(out_ref.dtype)


def features_t(states, lanes=256):
    rank, snaps = states.shape
    width = rank + rank * (rank + 1) // 2
    return pl.pallas_call(
        feature_kernel,
        grid=(snaps // lanes,),
        in_specs=[pl.BlockSpec((rank, lanes), lambda j: (0, j))],
        out_specs=pl.BlockSpec((width, lanes), lambda j: (0, j)),
        out_shape=jax.ShapeDtypeStruct((width, snaps), jnp.bfloat16),
        scratch_shapes=[pltpu.VMEM((width, lanes), jnp.float32)],
        cost_estimate=pl.CostEstimate(
            flops=width * snaps, transcendentals=0, bytes_accessed=rank * snaps * 4 + width * snaps * 2
        ),
    )(states)


def per_device(snapshots, basis):
    partial_value = lax.dot_general(
        basis, snapshots, (((0,), (0,)), ((), ())), preferred_element_type=jnp.float32
    )
    rank, columns = partial_value.shape
    groups = lax.axis_size("space")
    snaps = lax.axis_size("snap")
    received = lax.all_to_all(partial_value, "space", 0, 0, tiled=True)
    owned = jnp.sum(received, axis=0, keepdims=True)
    spread = jnp.broadcast_to(owned, (groups * snaps, columns))
    everyone = lax.all_to_all(spread, ("space", "snap"), 0, 0, tiled=True)
    states = everyone.reshape(rank, columns * snaps)
    total_snaps = states.shape[1]
    feats = features_t(states)
    targets = (jnp.roll(states, -1, axis=1) - states).astype(jnp.bfloat16)
    width = feats.shape[0]
    block_rows = width // snaps
    chosen = lax.dynamic_slice_in_dim(feats, lax.axis_index("snap") * block_rows, block_rows, 0)
    dims = (((1,), (1,)), ((), ()))
    normal = lax.dot_general(chosen, feats, dims, preferred_element_type=jnp.float32) / total_snaps
    rhs = lax.dot_general(chosen, targets, dims, preferred_element_type=jnp.float32) / total_snaps
    return (normal, rhs)


def solution(mesh):
    return jax.shard_map(
        per_device,
        mesh=mesh,
        in_specs=(P("space", "snap"), P("space", None)),
        out_specs=(P("snap", None), P("snap", None)),
        check_vma=False,
    )
```

```python
import jax
import jax.numpy as jnp
import numpy as np
from jax import lax
from jax.experimental import pallas as pl
from jax.experimental.pallas import tpu as pltpu
from jax.sharding import PartitionSpec as P


def swapped(block, axis, distance):
    count = lax.axis_size(axis)
    return lax.ppermute(block, axis, [(i, i ^ distance) for i in range(count)])


def butterfly_sum(block, axis):
    distance = 1
    while distance < lax.axis_size(axis):
        block = block + swapped(block, axis, distance)
        distance *= 2
    return block


def butterfly_gather(block, axis):
    index = lax.axis_index(axis)
    distance = 1
    while distance < lax.axis_size(axis):
        other = swapped(block, axis, distance)
        low = (index // distance) % 2 == 0
        block = jnp.where(
            low,
            jnp.concatenate([block, other], axis=1),
            jnp.concatenate([other, block], axis=1),
        )
        distance *= 2
    return block


def feature_kernel(states_ref, out_ref, rows_ref):
    rank = states_ref.shape[0]
    rows_ref[0:rank, :] = states_ref[...]
    offset = rank
    for a in range(rank):
        count = rank - a
        rows_ref[offset : offset + count, :] = states_ref[a : a + 1, :] * states_ref[a:rank, :]
        offset += count
    out_ref[...] = rows_ref[...].astype(out_ref.dtype)


def features_t(states, lanes=256):
    rank, snaps = states.shape
    width = rank + rank * (rank + 1) // 2
    return pl.pallas_call(
        feature_kernel,
        grid=(snaps // lanes,),
        in_specs=[pl.BlockSpec((rank, lanes), lambda j: (0, j))],
        out_specs=pl.BlockSpec((width, lanes), lambda j: (0, j)),
        out_shape=jax.ShapeDtypeStruct((width, snaps), jnp.bfloat16),
        scratch_shapes=[pltpu.VMEM((width, lanes), jnp.float32)],
        cost_estimate=pl.CostEstimate(
            flops=width * snaps, transcendentals=0, bytes_accessed=rank * snaps * 4 + width * snaps * 2
        ),
    )(states)


def per_device(snapshots, basis):
    partial_value = lax.dot_general(
        basis, snapshots, (((0,), (0,)), ((), ())), preferred_element_type=jnp.float32
    )
    rank, columns = partial_value.shape
    groups = lax.axis_size("space")
    snaps = lax.axis_size("snap")
    received = lax.all_to_all(partial_value, "space", 0, 0, tiled=True)
    owned = jnp.sum(received, axis=0, keepdims=True)
    across = lax.all_to_all(jnp.broadcast_to(owned, (snaps, columns)), "snap", 0, 0, tiled=True)
    row = across.reshape(1, snaps * columns)
    everyone = lax.all_to_all(jnp.broadcast_to(row, (groups, snaps * columns)), "space", 0, 0, tiled=True)
    states = everyone.reshape(rank, columns * snaps)
    total_snaps = states.shape[1]
    feats = features_t(states)
    targets = (jnp.roll(states, -1, axis=1) - states).astype(jnp.bfloat16)
    width = feats.shape[0]
    block_rows = width // snaps
    chosen = lax.dynamic_slice_in_dim(feats, lax.axis_index("snap") * block_rows, block_rows, 0)
    dims = (((1,), (1,)), ((), ()))
    normal = lax.dot_general(chosen, feats, dims, preferred_element_type=jnp.float32) / total_snaps
    rhs = lax.dot_general(chosen, targets, dims, preferred_element_type=jnp.float32) / total_snaps
    return (normal, rhs)


def solution(mesh):
    return jax.shard_map(
        per_device,
        mesh=mesh,
        in_specs=(P("space", "snap"), P("space", None)),
        out_specs=(P("snap", None), P("snap", None)),
        check_vma=False,
    )
```

```python
import functools

import jax
import jax.numpy as jnp
import numpy as np
from jax import lax
from jax.experimental import pallas as pl
from jax.experimental.pallas import tpu as pltpu
from jax.sharding import PartitionSpec as P


def swapped(block, axis, distance):
    count = lax.axis_size(axis)
    return lax.ppermute(block, axis, [(i, i ^ distance) for i in range(count)])


def butterfly_sum(block, axis):
    distance = 1
    while distance < lax.axis_size(axis):
        block = block + swapped(block, axis, distance)
        distance *= 2
    return block


def butterfly_gather(block, axis):
    index = lax.axis_index(axis)
    distance = 1
    while distance < lax.axis_size(axis):
        other = swapped(block, axis, distance)
        low = (index // distance) % 2 == 0
        block = jnp.where(
            low,
            jnp.concatenate([block, other], axis=1),
            jnp.concatenate([other, block], axis=1),
        )
        distance *= 2
    return block


def fill_rows(states_ref, rows_ref):
    rank = states_ref.shape[0]
    rows_ref[0:rank, :] = states_ref[...]
    offset = rank
    for a in range(rank):
        count = rank - a
        rows_ref[offset : offset + count, :] = states_ref[a : a + 1, :] * states_ref[a:rank, :]
        offset += count


def normal_kernel(first, count, scale, states_ref, targets_ref, normal_ref, rhs_ref, rows_ref):
    step = pl.program_id(0)
    fill_rows(states_ref, rows_ref)
    feats = rows_ref[...].astype(jnp.bfloat16)
    chosen = rows_ref[first : first + count, :].astype(jnp.bfloat16)
    dims = (((1,), (1,)), ((), ()))
    normal_part = lax.dot_general(chosen, feats, dims, preferred_element_type=jnp.float32)
    rhs_part = lax.dot_general(chosen, targets_ref[...], dims, preferred_element_type=jnp.float32)

    @pl.when(step == 0)
    def _():
        normal_ref[...] = normal_part
        rhs_ref[...] = rhs_part

    @pl.when(step > 0)
    def _():
        normal_ref[...] += normal_part
        rhs_ref[...] += rhs_part

    @pl.when(step == pl.num_programs(0) - 1)
    def _():
        normal_ref[...] = normal_ref[...] / scale
        rhs_ref[...] = rhs_ref[...] / scale


def normal_block(states, targets, block, blocks, lanes=256):
    rank, snaps = states.shape
    width = rank + rank * (rank + 1) // 2
    count = width // blocks
    kernel = functools.partial(normal_kernel, block * count, count, float(snaps))
    return pl.pallas_call(
        kernel,
        grid=(snaps // lanes,),
        in_specs=[
            pl.BlockSpec((rank, lanes), lambda j: (0, j)),
            pl.BlockSpec((rank, lanes), lambda j: (0, j)),
        ],
        out_specs=[
            pl.BlockSpec((count, width), lambda j: (0, 0)),
            pl.BlockSpec((count, rank), lambda j: (0, 0)),
        ],
        out_shape=[
            jax.ShapeDtypeStruct((count, width), jnp.float32),
            jax.ShapeDtypeStruct((count, rank), jnp.float32),
        ],
        scratch_shapes=[pltpu.VMEM((width, lanes), jnp.float32)],
        compiler_params=pltpu.CompilerParams(vmem_limit_bytes=48 * 1024 * 1024),
        cost_estimate=pl.CostEstimate(
            flops=2 * count * (width + rank) * snaps,
            transcendentals=0,
            bytes_accessed=rank * snaps * 6 + count * (width + rank) * 4,
        ),
    )(states, targets)


def per_device(snapshots, basis):
    partial_value = lax.dot_general(
        basis, snapshots, (((0,), (0,)), ((), ())), preferred_element_type=jnp.float32
    )
    rank, columns = partial_value.shape
    groups = lax.axis_size("space")
    snaps = lax.axis_size("snap")
    received = lax.all_to_all(partial_value, "space", 0, 0, tiled=True)
    owned = jnp.sum(received, axis=0, keepdims=True)
    spread = jnp.broadcast_to(owned, (groups * snaps, columns))
    everyone = lax.all_to_all(spread, ("space", "snap"), 0, 0, tiled=True)
    states = everyone.reshape(rank, columns * snaps)
    targets = (jnp.roll(states, -1, axis=1) - states).astype(jnp.bfloat16)
    branches = [functools.partial(normal_block, block=b, blocks=snaps) for b in range(snaps)]
    normal, rhs = lax.switch(lax.axis_index("snap"), branches, states, targets)
    return (normal, rhs)


def solution(mesh):
    return jax.shard_map(
        per_device,
        mesh=mesh,
        in_specs=(P("space", "snap"), P("space", None)),
        out_specs=(P("snap", None), P("snap", None)),
        check_vma=False,
    )
```

```python
import functools

import jax
import jax.numpy as jnp
import numpy as np
from jax import lax
from jax.experimental import pallas as pl
from jax.experimental.pallas import tpu as pltpu
from jax.sharding import PartitionSpec as P


def swapped(block, axis, distance):
    count = lax.axis_size(axis)
    return lax.ppermute(block, axis, [(i, i ^ distance) for i in range(count)])


def butterfly_sum(block, axis):
    distance = 1
    while distance < lax.axis_size(axis):
        block = block + swapped(block, axis, distance)
        distance *= 2
    return block


def butterfly_gather(block, axis):
    index = lax.axis_index(axis)
    distance = 1
    while distance < lax.axis_size(axis):
        other = swapped(block, axis, distance)
        low = (index // distance) % 2 == 0
        block = jnp.where(
            low,
            jnp.concatenate([block, other], axis=1),
            jnp.concatenate([other, block], axis=1),
        )
        distance *= 2
    return block


def fill_rows(states_ref, rows_ref):
    rank = states_ref.shape[0]
    rows_ref[0:rank, :] = states_ref[...]
    offset = rank
    for a in range(rank):
        count = rank - a
        rows_ref[offset : offset + count, :] = states_ref[a : a + 1, :] * states_ref[a:rank, :]
        offset += count


def normal_kernel(first, count, scale, states_ref, targets_ref, normal_ref, rhs_ref, rows_ref):
    step = pl.program_id(0)
    fill_rows(states_ref, rows_ref)
    feats = rows_ref[...].astype(jnp.bfloat16)
    chosen = rows_ref[first : first + count, :].astype(jnp.bfloat16)
    dims = (((1,), (1,)), ((), ()))
    normal_part = lax.dot_general(chosen, feats, dims, preferred_element_type=jnp.float32)
    rhs_part = lax.dot_general(chosen, targets_ref[...], dims, preferred_element_type=jnp.float32)

    @pl.when(step == 0)
    def _():
        normal_ref[...] = normal_part
        rhs_ref[...] = rhs_part

    @pl.when(step > 0)
    def _():
        normal_ref[...] += normal_part
        rhs_ref[...] += rhs_part

    @pl.when(step == pl.num_programs(0) - 1)
    def _():
        normal_ref[...] = normal_ref[...] / scale
        rhs_ref[...] = rhs_ref[...] / scale


def normal_block(states, targets, block, blocks, lanes=1024):
    rank, snaps = states.shape
    width = rank + rank * (rank + 1) // 2
    count = width // blocks
    kernel = functools.partial(normal_kernel, block * count, count, float(snaps))
    return pl.pallas_call(
        kernel,
        grid=(snaps // lanes,),
        in_specs=[
            pl.BlockSpec((rank, lanes), lambda j: (0, j)),
            pl.BlockSpec((rank, lanes), lambda j: (0, j)),
        ],
        out_specs=[
            pl.BlockSpec((count, width), lambda j: (0, 0)),
            pl.BlockSpec((count, rank), lambda j: (0, 0)),
        ],
        out_shape=[
            jax.ShapeDtypeStruct((count, width), jnp.float32),
            jax.ShapeDtypeStruct((count, rank), jnp.float32),
        ],
        scratch_shapes=[pltpu.VMEM((width, lanes), jnp.float32)],
        compiler_params=pltpu.CompilerParams(vmem_limit_bytes=48 * 1024 * 1024),
        cost_estimate=pl.CostEstimate(
            flops=2 * count * (width + rank) * snaps,
            transcendentals=0,
            bytes_accessed=rank * snaps * 6 + count * (width + rank) * 4,
        ),
    )(states, targets)


def per_device(snapshots, basis):
    partial_value = lax.dot_general(
        basis, snapshots, (((0,), (0,)), ((), ())), preferred_element_type=jnp.float32
    )
    rank, columns = partial_value.shape
    groups = lax.axis_size("space")
    snaps = lax.axis_size("snap")
    received = lax.all_to_all(partial_value, "space", 0, 0, tiled=True)
    owned = jnp.sum(received, axis=0, keepdims=True)
    spread = jnp.broadcast_to(owned, (groups * snaps, columns))
    everyone = lax.all_to_all(spread, ("space", "snap"), 0, 0, tiled=True)
    states = everyone.reshape(rank, columns * snaps)
    targets = (jnp.roll(states, -1, axis=1) - states).astype(jnp.bfloat16)
    branches = [functools.partial(normal_block, block=b, blocks=snaps) for b in range(snaps)]
    normal, rhs = lax.switch(lax.axis_index("snap"), branches, states, targets)
    return (normal, rhs)


def solution(mesh):
    return jax.shard_map(
        per_device,
        mesh=mesh,
        in_specs=(P("space", "snap"), P("space", None)),
        out_specs=(P("snap", None), P("snap", None)),
        check_vma=False,
    )
```

```python
import functools

import jax
import jax.numpy as jnp
import numpy as np
from jax import lax
from jax.experimental import pallas as pl
from jax.experimental.pallas import tpu as pltpu
from jax.sharding import PartitionSpec as P


def swapped(block, axis, distance):
    count = lax.axis_size(axis)
    return lax.ppermute(block, axis, [(i, i ^ distance) for i in range(count)])


def butterfly_sum(block, axis):
    distance = 1
    while distance < lax.axis_size(axis):
        block = block + swapped(block, axis, distance)
        distance *= 2
    return block


def butterfly_gather(block, axis):
    index = lax.axis_index(axis)
    distance = 1
    while distance < lax.axis_size(axis):
        other = swapped(block, axis, distance)
        low = (index // distance) % 2 == 0
        block = jnp.where(
            low,
            jnp.concatenate([block, other], axis=1),
            jnp.concatenate([other, block], axis=1),
        )
        distance *= 2
    return block


def fill_rows(states_ref, rows_ref):
    rank = states_ref.shape[0]
    rows_ref[0:rank, :] = states_ref[...]
    offset = rank
    for a in range(rank):
        count = rank - a
        rows_ref[offset : offset + count, :] = states_ref[a : a + 1, :] * states_ref[a:rank, :]
        offset += count


def normal_kernel(first, count, scale, states_ref, targets_ref, normal_ref, rhs_ref, rows_ref):
    step = pl.program_id(0)
    fill_rows(states_ref, rows_ref)
    feats = rows_ref[...].astype(jnp.bfloat16)
    chosen = rows_ref[first : first + count, :].astype(jnp.bfloat16)
    dims = (((1,), (1,)), ((), ()))
    normal_part = lax.dot_general(chosen, feats, dims, preferred_element_type=jnp.float32)
    rhs_part = lax.dot_general(chosen, targets_ref[...], dims, preferred_element_type=jnp.float32)

    @pl.when(step == 0)
    def _():
        normal_ref[...] = normal_part
        rhs_ref[...] = rhs_part

    @pl.when(step > 0)
    def _():
        normal_ref[...] += normal_part
        rhs_ref[...] += rhs_part

    @pl.when(step == pl.num_programs(0) - 1)
    def _():
        normal_ref[...] = normal_ref[...] / scale
        rhs_ref[...] = rhs_ref[...] / scale


def normal_block(states, targets, block, blocks, lanes=1024):
    rank, snaps = states.shape
    width = rank + rank * (rank + 1) // 2
    count = width // blocks
    kernel = functools.partial(normal_kernel, block * count, count, float(snaps))
    return pl.pallas_call(
        kernel,
        grid=(snaps // lanes,),
        in_specs=[
            pl.BlockSpec((rank, lanes), lambda j: (0, j)),
            pl.BlockSpec((rank, lanes), lambda j: (0, j)),
        ],
        out_specs=[
            pl.BlockSpec((count, width), lambda j: (0, 0)),
            pl.BlockSpec((count, rank), lambda j: (0, 0)),
        ],
        out_shape=[
            jax.ShapeDtypeStruct((count, width), jnp.float32),
            jax.ShapeDtypeStruct((count, rank), jnp.float32),
        ],
        scratch_shapes=[pltpu.VMEM((width, lanes), jnp.float32)],
        compiler_params=pltpu.CompilerParams(vmem_limit_bytes=48 * 1024 * 1024),
        cost_estimate=pl.CostEstimate(
            flops=2 * count * (width + rank) * snaps,
            transcendentals=0,
            bytes_accessed=rank * snaps * 6 + count * (width + rank) * 4,
        ),
    )(states, targets)


def per_device(snapshots, basis):
    partial_value = lax.dot_general(
        basis, snapshots, (((0,), (0,)), ((), ())), preferred_element_type=jnp.float32
    )
    rank, columns = partial_value.shape
    chips = lax.axis_size("chip")
    cores = lax.axis_size("core")
    snaps = lax.axis_size("snap")
    core = lax.axis_index("core")
    by_chip = partial_value.reshape(cores, chips, columns).transpose(1, 0, 2).reshape(rank, columns)
    received = lax.all_to_all(by_chip, ("chip", "core"), 0, 0, tiled=True)
    owned = jnp.sum(received, axis=0, keepdims=True)
    spread = jnp.broadcast_to(owned, (chips * snaps, columns))
    half = lax.all_to_all(spread, ("chip", "snap"), 0, 0, tiled=True).reshape(chips, snaps * columns)
    other = lax.ppermute(half, "core", [(0, 1), (1, 0)])
    states = jnp.where(
        core == 0,
        jnp.concatenate([half, other], axis=0),
        jnp.concatenate([other, half], axis=0),
    )
    targets = (jnp.roll(states, -1, axis=1) - states).astype(jnp.bfloat16)
    branches = [functools.partial(normal_block, block=b, blocks=snaps) for b in range(snaps)]
    normal, rhs = lax.switch(lax.axis_index("snap"), branches, states, targets)
    return (normal, rhs)


def solution(mesh):
    space, snaps = mesh.devices.shape
    chip_mesh = jax.sharding.Mesh(
        mesh.devices.reshape(space // 2, 2, snaps), ("chip", "core", mesh.axis_names[1])
    )
    return jax.shard_map(
        per_device,
        mesh=chip_mesh,
        in_specs=(P(("chip", "core"), "snap"), P(("chip", "core"), None)),
        out_specs=(P("snap", None), P("snap", None)),
        check_vma=False,
    )
```

```python
import functools

import jax
import jax.numpy as jnp
import numpy as np
from jax import lax
from jax.experimental import pallas as pl
from jax.experimental.pallas import tpu as pltpu
from jax.sharding import PartitionSpec as P


def swapped(block, axis, distance):
    count = lax.axis_size(axis)
    return lax.ppermute(block, axis, [(i, i ^ distance) for i in range(count)])


def butterfly_sum(block, axis):
    distance = 1
    while distance < lax.axis_size(axis):
        block = block + swapped(block, axis, distance)
        distance *= 2
    return block


def butterfly_gather(block, axis):
    index = lax.axis_index(axis)
    distance = 1
    while distance < lax.axis_size(axis):
        other = swapped(block, axis, distance)
        low = (index // distance) % 2 == 0
        block = jnp.where(
            low,
            jnp.concatenate([block, other], axis=1),
            jnp.concatenate([other, block], axis=1),
        )
        distance *= 2
    return block


def fill_rows(states_ref, rows_ref):
    rank = states_ref.shape[0]
    rows_ref[0:rank, :] = states_ref[...]
    offset = rank
    for a in range(rank):
        count = rank - a
        rows_ref[offset : offset + count, :] = states_ref[a : a + 1, :] * states_ref[a:rank, :]
        offset += count


def normal_kernel(first, count, scale, states_ref, targets_ref, normal_ref, rhs_ref, rows_ref):
    step = pl.program_id(0)
    fill_rows(states_ref, rows_ref)
    feats = rows_ref[...].astype(jnp.bfloat16)
    chosen = rows_ref[first : first + count, :].astype(jnp.bfloat16)
    dims = (((1,), (1,)), ((), ()))
    normal_part = lax.dot_general(chosen, feats, dims, preferred_element_type=jnp.float32)
    rhs_part = lax.dot_general(chosen, targets_ref[...], dims, preferred_element_type=jnp.float32)

    @pl.when(step == 0)
    def _():
        normal_ref[...] = normal_part
        rhs_ref[...] = rhs_part

    @pl.when(step > 0)
    def _():
        normal_ref[...] += normal_part
        rhs_ref[...] += rhs_part

    @pl.when(step == pl.num_programs(0) - 1)
    def _():
        normal_ref[...] = normal_ref[...] / scale
        rhs_ref[...] = rhs_ref[...] / scale


def normal_block(states, targets, block, blocks, lanes=2048):
    rank, snaps = states.shape
    width = rank + rank * (rank + 1) // 2
    count = width // blocks
    kernel = functools.partial(normal_kernel, block * count, count, float(snaps))
    return pl.pallas_call(
        kernel,
        grid=(snaps // lanes,),
        in_specs=[
            pl.BlockSpec((rank, lanes), lambda j: (0, j)),
            pl.BlockSpec((rank, lanes), lambda j: (0, j)),
        ],
        out_specs=[
            pl.BlockSpec((count, width), lambda j: (0, 0)),
            pl.BlockSpec((count, rank), lambda j: (0, 0)),
        ],
        out_shape=[
            jax.ShapeDtypeStruct((count, width), jnp.float32),
            jax.ShapeDtypeStruct((count, rank), jnp.float32),
        ],
        scratch_shapes=[pltpu.VMEM((width, lanes), jnp.float32)],
        compiler_params=pltpu.CompilerParams(vmem_limit_bytes=48 * 1024 * 1024),
        cost_estimate=pl.CostEstimate(
            flops=2 * count * (width + rank) * snaps,
            transcendentals=0,
            bytes_accessed=rank * snaps * 6 + count * (width + rank) * 4,
        ),
    )(states, targets)


def project_kernel(basis_ref, snapshots_ref, out_ref):
    part = lax.dot_general(
        basis_ref[...], snapshots_ref[...], (((0,), (0,)), ((), ())), preferred_element_type=jnp.float32
    )

    @pl.when(pl.program_id(0) == 0)
    def _():
        out_ref[...] = part

    @pl.when(pl.program_id(0) > 0)
    def _():
        out_ref[...] += part


def project(basis, snapshots, depth=512):
    rows, rank = basis.shape
    columns = snapshots.shape[1]
    return pl.pallas_call(
        project_kernel,
        grid=(rows // depth,),
        in_specs=[
            pl.BlockSpec((depth, rank), lambda k: (k, 0)),
            pl.BlockSpec((depth, columns), lambda k: (k, 0)),
        ],
        out_specs=pl.BlockSpec((rank, columns), lambda k: (0, 0)),
        out_shape=jax.ShapeDtypeStruct((rank, columns), jnp.float32),
        cost_estimate=pl.CostEstimate(
            flops=2 * rows * rank * columns,
            transcendentals=0,
            bytes_accessed=rows * (rank + columns) * 2 + rank * columns * 4,
        ),
    )(basis, snapshots)


def per_device(snapshots, basis):
    partial_value = project(basis, snapshots)
    rank, columns = partial_value.shape
    chips = lax.axis_size("chip")
    cores = lax.axis_size("core")
    snaps = lax.axis_size("snap")
    core = lax.axis_index("core")
    by_chip = partial_value.reshape(cores, chips, columns).transpose(1, 0, 2).reshape(rank, columns)
    received = lax.all_to_all(by_chip, ("chip", "core"), 0, 0, tiled=True)
    owned = jnp.sum(received, axis=0, keepdims=True)
    spread = jnp.broadcast_to(owned, (chips * snaps, columns))
    half = lax.all_to_all(spread, ("chip", "snap"), 0, 0, tiled=True).reshape(chips, snaps * columns)
    other = lax.ppermute(half, "core", [(0, 1), (1, 0)])
    states = jnp.where(
        core == 0,
        jnp.concatenate([half, other], axis=0),
        jnp.concatenate([other, half], axis=0),
    )
    targets = (jnp.roll(states, -1, axis=1) - states).astype(jnp.bfloat16)
    branches = [functools.partial(normal_block, block=b, blocks=snaps) for b in range(snaps)]
    normal, rhs = lax.switch(lax.axis_index("snap"), branches, states, targets)
    return (normal, rhs)


def solution(mesh):
    space, snaps = mesh.devices.shape
    chip_mesh = jax.sharding.Mesh(
        mesh.devices.reshape(space // 2, 2, snaps), ("chip", "core", mesh.axis_names[1])
    )
    return jax.shard_map(
        per_device,
        mesh=chip_mesh,
        in_specs=(P(("chip", "core"), "snap"), P(("chip", "core"), None)),
        out_specs=(P("snap", None), P("snap", None)),
        check_vma=False,
    )
```

```python
import functools

import jax
import jax.numpy as jnp
import numpy as np
from jax import lax
from jax.experimental import pallas as pl
from jax.experimental.pallas import tpu as pltpu
from jax.sharding import PartitionSpec as P


def swapped(block, axis, distance):
    count = lax.axis_size(axis)
    return lax.ppermute(block, axis, [(i, i ^ distance) for i in range(count)])


def butterfly_sum(block, axis):
    distance = 1
    while distance < lax.axis_size(axis):
        block = block + swapped(block, axis, distance)
        distance *= 2
    return block


def butterfly_gather(block, axis):
    index = lax.axis_index(axis)
    distance = 1
    while distance < lax.axis_size(axis):
        other = swapped(block, axis, distance)
        low = (index // distance) % 2 == 0
        block = jnp.where(
            low,
            jnp.concatenate([block, other], axis=1),
            jnp.concatenate([other, block], axis=1),
        )
        distance *= 2
    return block


def fill_rows(states_ref, rows_ref):
    rank = states_ref.shape[0]
    rows_ref[0:rank, :] = states_ref[...]
    offset = rank
    for a in range(rank):
        count = rank - a
        rows_ref[offset : offset + count, :] = states_ref[a : a + 1, :] * states_ref[a:rank, :]
        offset += count


def normal_kernel(count, scale, block_ref, states_ref, targets_ref, normal_ref, rhs_ref, rows_ref):
    fill_rows(states_ref, rows_ref)
    feats = rows_ref[...].astype(jnp.bfloat16)
    first = block_ref[0] * count
    window = count + (-count) % 8
    aligned = pl.multiple_of((first // 8) * 8, 8)
    lifted = rows_ref[pl.ds(aligned, window), :]
    shift = (window - (first - aligned)) % window
    chosen = pltpu.roll(lifted, shift, 0)[0:count, :].astype(jnp.bfloat16)
    dims = (((1,), (1,)), ((), ()))
    normal_part = lax.dot_general(chosen, feats, dims, preferred_element_type=jnp.float32)
    rhs_part = lax.dot_general(chosen, targets_ref[...], dims, preferred_element_type=jnp.float32)
    normal_ref[...] = normal_part / scale
    rhs_ref[...] = rhs_part / scale


def normal_block(states, targets, block, blocks):
    rank, snaps = states.shape
    width = rank + rank * (rank + 1) // 2
    count = width // blocks
    kernel = functools.partial(normal_kernel, count, float(snaps))
    return pl.pallas_call(
        kernel,
        grid_spec=pltpu.PrefetchScalarGridSpec(
            num_scalar_prefetch=1,
            grid=(1,),
            in_specs=[
                pl.BlockSpec((rank, snaps), lambda j, b: (0, 0)),
                pl.BlockSpec((rank, snaps), lambda j, b: (0, 0)),
            ],
            out_specs=[
                pl.BlockSpec((count, width), lambda j, b: (0, 0)),
                pl.BlockSpec((count, rank), lambda j, b: (0, 0)),
            ],
            scratch_shapes=[pltpu.VMEM((width, snaps), jnp.float32)],
        ),
        out_shape=[
            jax.ShapeDtypeStruct((count, width), jnp.float32),
            jax.ShapeDtypeStruct((count, rank), jnp.float32),
        ],
        compiler_params=pltpu.CompilerParams(vmem_limit_bytes=48 * 1024 * 1024),
        cost_estimate=pl.CostEstimate(
            flops=2 * count * (width + rank) * snaps,
            transcendentals=0,
            bytes_accessed=rank * snaps * 6 + count * (width + rank) * 4,
        ),
    )(jnp.reshape(block, (1,)).astype(jnp.int32), states, targets)


def per_device(snapshots, basis):
    partial_value = lax.dot_general(
        basis, snapshots, (((0,), (0,)), ((), ())), preferred_element_type=jnp.float32
    )
    rank, columns = partial_value.shape
    chips = lax.axis_size("chip")
    cores = lax.axis_size("core")
    snaps = lax.axis_size("snap")
    core = lax.axis_index("core")
    by_chip = partial_value.reshape(cores, chips, columns).transpose(1, 0, 2).reshape(rank, columns)
    received = lax.all_to_all(by_chip, ("chip", "core"), 0, 0, tiled=True)
    owned = jnp.sum(received, axis=0, keepdims=True)
    spread = jnp.broadcast_to(owned, (chips * snaps, columns))
    half = lax.all_to_all(spread, ("chip", "snap"), 0, 0, tiled=True).reshape(chips, snaps * columns)
    other = lax.ppermute(half, "core", [(0, 1), (1, 0)])
    states = jnp.where(
        core == 0,
        jnp.concatenate([half, other], axis=0),
        jnp.concatenate([other, half], axis=0),
    )
    targets = (jnp.roll(states, -1, axis=1) - states).astype(jnp.bfloat16)
    normal, rhs = normal_block(states, targets, lax.axis_index("snap"), snaps)
    return (normal, rhs)


def solution(mesh):
    space, snaps = mesh.devices.shape
    chip_mesh = jax.sharding.Mesh(
        mesh.devices.reshape(space // 2, 2, snaps), ("chip", "core", mesh.axis_names[1])
    )
    return jax.shard_map(
        per_device,
        mesh=chip_mesh,
        in_specs=(P(("chip", "core"), "snap"), P(("chip", "core"), None)),
        out_specs=(P("snap", None), P("snap", None)),
        check_vma=False,
    )
```

```python
import functools

import jax
import jax.numpy as jnp
import numpy as np
from jax import lax
from jax.experimental import pallas as pl
from jax.experimental.pallas import tpu as pltpu
from jax.sharding import PartitionSpec as P


def swapped(block, axis, distance):
    count = lax.axis_size(axis)
    return lax.ppermute(block, axis, [(i, i ^ distance) for i in range(count)])


def butterfly_sum(block, axis):
    distance = 1
    while distance < lax.axis_size(axis):
        block = block + swapped(block, axis, distance)
        distance *= 2
    return block


def butterfly_gather(block, axis):
    index = lax.axis_index(axis)
    distance = 1
    while distance < lax.axis_size(axis):
        other = swapped(block, axis, distance)
        low = (index // distance) % 2 == 0
        block = jnp.where(
            low,
            jnp.concatenate([block, other], axis=1),
            jnp.concatenate([other, block], axis=1),
        )
        distance *= 2
    return block


def fill_rows(states_ref, rows_ref):
    rank = states_ref.shape[0]
    rows_ref[0:rank, :] = states_ref[...]
    offset = rank
    for a in range(rank):
        count = rank - a
        rows_ref[offset : offset + count, :] = states_ref[a : a + 1, :] * states_ref[a:rank, :]
        offset += count


def normal_kernel(first, count, scale, states_ref, targets_ref, normal_ref, rhs_ref, rows_ref):
    step = pl.program_id(0)
    fill_rows(states_ref, rows_ref)
    feats = rows_ref[...].astype(jnp.bfloat16)
    chosen = rows_ref[first : first + count, :].astype(jnp.bfloat16)
    dims = (((1,), (1,)), ((), ()))
    normal_part = lax.dot_general(chosen, feats, dims, preferred_element_type=jnp.float32)
    rhs_part = lax.dot_general(chosen, targets_ref[...], dims, preferred_element_type=jnp.float32)

    @pl.when(step == 0)
    def _():
        normal_ref[...] = normal_part
        rhs_ref[...] = rhs_part

    @pl.when(step > 0)
    def _():
        normal_ref[...] += normal_part
        rhs_ref[...] += rhs_part

    @pl.when(step == pl.num_programs(0) - 1)
    def _():
        normal_ref[...] = normal_ref[...] / scale
        rhs_ref[...] = rhs_ref[...] / scale


def normal_block(states, targets, block, blocks, lanes=2048):
    rank, snaps = states.shape
    width = rank + rank * (rank + 1) // 2
    count = width // blocks
    kernel = functools.partial(normal_kernel, block * count, count, float(snaps))
    return pl.pallas_call(
        kernel,
        grid=(snaps // lanes,),
        in_specs=[
            pl.BlockSpec((rank, lanes), lambda j: (0, j)),
            pl.BlockSpec((rank, lanes), lambda j: (0, j)),
        ],
        out_specs=[
            pl.BlockSpec((count, width), lambda j: (0, 0)),
            pl.BlockSpec((count, rank), lambda j: (0, 0)),
        ],
        out_shape=[
            jax.ShapeDtypeStruct((count, width), jnp.float32),
            jax.ShapeDtypeStruct((count, rank), jnp.float32),
        ],
        scratch_shapes=[pltpu.VMEM((width, lanes), jnp.float32)],
        compiler_params=pltpu.CompilerParams(vmem_limit_bytes=48 * 1024 * 1024),
        cost_estimate=pl.CostEstimate(
            flops=2 * count * (width + rank) * snaps,
            transcendentals=0,
            bytes_accessed=rank * snaps * 6 + count * (width + rank) * 4,
        ),
    )(states, targets)


def project_kernel(basis_ref, snapshots_ref, out_ref):
    part = jnp.dot(basis_ref[...], snapshots_ref[...], preferred_element_type=jnp.float32)

    @pl.when(pl.program_id(0) == 0)
    def _():
        out_ref[...] = part

    @pl.when(pl.program_id(0) > 0)
    def _():
        out_ref[...] += part


def project(basis_t, snapshots, depth=1024):
    rank, rows = basis_t.shape
    columns = snapshots.shape[1]
    return pl.pallas_call(
        project_kernel,
        grid=(rows // depth,),
        in_specs=[
            pl.BlockSpec((rank, depth), lambda k: (0, k)),
            pl.BlockSpec((depth, columns), lambda k: (k, 0)),
        ],
        out_specs=pl.BlockSpec((rank, columns), lambda k: (0, 0)),
        out_shape=jax.ShapeDtypeStruct((rank, columns), jnp.float32),
        cost_estimate=pl.CostEstimate(
            flops=2 * rows * rank * columns,
            transcendentals=0,
            bytes_accessed=rows * (rank + columns) * 2 + rank * columns * 4,
        ),
    )(basis_t, snapshots)


def per_device(snapshots, basis):
    partial_value = project(basis.T, snapshots)
    rank, columns = partial_value.shape
    chips = lax.axis_size("chip")
    cores = lax.axis_size("core")
    snaps = lax.axis_size("snap")
    core = lax.axis_index("core")
    by_chip = partial_value.reshape(cores, chips, columns).transpose(1, 0, 2).reshape(rank, columns)
    received = lax.all_to_all(by_chip, ("chip", "core"), 0, 0, tiled=True)
    owned = jnp.sum(received, axis=0, keepdims=True)
    spread = jnp.broadcast_to(owned, (chips * snaps, columns))
    half = lax.all_to_all(spread, ("chip", "snap"), 0, 0, tiled=True).reshape(chips, snaps * columns)
    other = lax.ppermute(half, "core", [(0, 1), (1, 0)])
    states = jnp.where(
        core == 0,
        jnp.concatenate([half, other], axis=0),
        jnp.concatenate([other, half], axis=0),
    )
    targets = (jnp.roll(states, -1, axis=1) - states).astype(jnp.bfloat16)
    branches = [functools.partial(normal_block, block=b, blocks=snaps) for b in range(snaps)]
    normal, rhs = lax.switch(lax.axis_index("snap"), branches, states, targets)
    return (normal, rhs)


def solution(mesh):
    space, snaps = mesh.devices.shape
    chip_mesh = jax.sharding.Mesh(
        mesh.devices.reshape(space // 2, 2, snaps), ("chip", "core", mesh.axis_names[1])
    )
    return jax.shard_map(
        per_device,
        mesh=chip_mesh,
        in_specs=(P(("chip", "core"), "snap"), P(("chip", "core"), None)),
        out_specs=(P("snap", None), P("snap", None)),
        check_vma=False,
    )
```

```python
import functools

import jax
import jax.numpy as jnp
import numpy as np
from jax import lax
from jax.experimental import pallas as pl
from jax.experimental.pallas import tpu as pltpu
from jax.sharding import PartitionSpec as P


def swapped(block, axis, distance):
    count = lax.axis_size(axis)
    return lax.ppermute(block, axis, [(i, i ^ distance) for i in range(count)])


def butterfly_sum(block, axis):
    distance = 1
    while distance < lax.axis_size(axis):
        block = block + swapped(block, axis, distance)
        distance *= 2
    return block


def butterfly_gather(block, axis):
    index = lax.axis_index(axis)
    distance = 1
    while distance < lax.axis_size(axis):
        other = swapped(block, axis, distance)
        low = (index // distance) % 2 == 0
        block = jnp.where(
            low,
            jnp.concatenate([block, other], axis=1),
            jnp.concatenate([other, block], axis=1),
        )
        distance *= 2
    return block


def fill_rows(states_ref, rows_ref):
    rank = states_ref.shape[0]
    rows_ref[0:rank, :] = states_ref[...]
    offset = rank
    for a in range(rank):
        count = rank - a
        rows_ref[offset : offset + count, :] = states_ref[a : a + 1, :] * states_ref[a:rank, :]
        offset += count


def normal_kernel(first, count, scale, states_ref, targets_ref, normal_ref, rhs_ref, rows_ref):
    step = pl.program_id(0)
    fill_rows(states_ref, rows_ref)
    feats = rows_ref[...].astype(jnp.bfloat16)
    chosen = rows_ref[first : first + count, :].astype(jnp.bfloat16)
    dims = (((1,), (1,)), ((), ()))
    normal_part = lax.dot_general(chosen, feats, dims, preferred_element_type=jnp.float32)
    rhs_part = lax.dot_general(targets_ref[...], chosen, dims, preferred_element_type=jnp.float32)

    @pl.when(step == 0)
    def _():
        normal_ref[...] = normal_part
        rhs_ref[...] = rhs_part

    @pl.when(step > 0)
    def _():
        normal_ref[...] += normal_part
        rhs_ref[...] += rhs_part

    @pl.when(step == pl.num_programs(0) - 1)
    def _():
        normal_ref[...] = normal_ref[...] / scale
        rhs_ref[...] = rhs_ref[...] / scale


def normal_block(states, targets, block, blocks, lanes=2048):
    rank, snaps = states.shape
    width = rank + rank * (rank + 1) // 2
    count = width // blocks
    kernel = functools.partial(normal_kernel, block * count, count, float(snaps))
    return pl.pallas_call(
        kernel,
        grid=(snaps // lanes,),
        in_specs=[
            pl.BlockSpec((rank, lanes), lambda j: (0, j)),
            pl.BlockSpec((rank, lanes), lambda j: (0, j)),
        ],
        out_specs=[
            pl.BlockSpec((count, width), lambda j: (0, 0)),
            pl.BlockSpec((rank, count), lambda j: (0, 0)),
        ],
        out_shape=[
            jax.ShapeDtypeStruct((count, width), jnp.float32),
            jax.ShapeDtypeStruct((rank, count), jnp.float32),
        ],
        scratch_shapes=[pltpu.VMEM((width, lanes), jnp.float32)],
        compiler_params=pltpu.CompilerParams(vmem_limit_bytes=48 * 1024 * 1024),
        cost_estimate=pl.CostEstimate(
            flops=2 * count * (width + rank) * snaps,
            transcendentals=0,
            bytes_accessed=rank * snaps * 6 + count * (width + rank) * 4,
        ),
    )(states, targets)


def per_device(snapshots, basis):
    partial_value = lax.dot_general(
        basis, snapshots, (((0,), (0,)), ((), ())), preferred_element_type=jnp.float32
    )
    rank, columns = partial_value.shape
    chips = lax.axis_size("chip")
    cores = lax.axis_size("core")
    snaps = lax.axis_size("snap")
    core = lax.axis_index("core")
    by_chip = partial_value.reshape(cores, chips, columns).transpose(1, 0, 2).reshape(rank, columns)
    received = lax.all_to_all(by_chip, ("chip", "core"), 0, 0, tiled=True)
    owned = jnp.sum(received, axis=0, keepdims=True)
    spread = jnp.broadcast_to(owned, (chips * snaps, columns))
    half = lax.all_to_all(spread, ("chip", "snap"), 0, 0, tiled=True).reshape(chips, snaps * columns)
    other = lax.ppermute(half, "core", [(0, 1), (1, 0)])
    states = jnp.where(
        core == 0,
        jnp.concatenate([half, other], axis=0),
        jnp.concatenate([other, half], axis=0),
    )
    targets = (jnp.roll(states, -1, axis=1) - states).astype(jnp.bfloat16)
    branches = [functools.partial(normal_block, block=b, blocks=snaps) for b in range(snaps)]
    normal, rhs_t = lax.switch(lax.axis_index("snap"), branches, states, targets)
    return (normal, rhs_t.T)


def solution(mesh):
    space, snaps = mesh.devices.shape
    chip_mesh = jax.sharding.Mesh(
        mesh.devices.reshape(space // 2, 2, snaps), ("chip", "core", mesh.axis_names[1])
    )
    return jax.shard_map(
        per_device,
        mesh=chip_mesh,
        in_specs=(P(("chip", "core"), "snap"), P(("chip", "core"), None)),
        out_specs=(P("snap", None), P("snap", None)),
        check_vma=False,
    )
```

```python
import functools

import jax
import jax.numpy as jnp
import numpy as np
from jax import lax
from jax.experimental import pallas as pl
from jax.experimental.pallas import tpu as pltpu
from jax.sharding import PartitionSpec as P


def swapped(block, axis, distance):
    count = lax.axis_size(axis)
    return lax.ppermute(block, axis, [(i, i ^ distance) for i in range(count)])


def butterfly_sum(block, axis):
    distance = 1
    while distance < lax.axis_size(axis):
        block = block + swapped(block, axis, distance)
        distance *= 2
    return block


def butterfly_gather(block, axis):
    index = lax.axis_index(axis)
    distance = 1
    while distance < lax.axis_size(axis):
        other = swapped(block, axis, distance)
        low = (index // distance) % 2 == 0
        block = jnp.where(
            low,
            jnp.concatenate([block, other], axis=1),
            jnp.concatenate([other, block], axis=1),
        )
        distance *= 2
    return block


def fill_rows(states_ref, rows_ref):
    rank = states_ref.shape[0]
    rows_ref[0:rank, :] = states_ref[...]
    offset = rank
    for a in range(rank):
        count = rank - a
        rows_ref[offset : offset + count, :] = states_ref[a : a + 1, :] * states_ref[a:rank, :]
        offset += count


def normal_kernel(first, count, scale, states_ref, targets_ref, normal_ref, rhs_ref, rows_ref):
    step = pl.program_id(0)
    fill_rows(states_ref, rows_ref)
    feats = rows_ref[...].astype(jnp.bfloat16)
    chosen = rows_ref[first : first + count, :].astype(jnp.bfloat16)
    dims = (((1,), (1,)), ((), ()))
    normal_part = lax.dot_general(chosen, feats, dims, preferred_element_type=jnp.float32)
    rhs_part = lax.dot_general(targets_ref[...], chosen, dims, preferred_element_type=jnp.float32)

    @pl.when(step == 0)
    def _():
        normal_ref[...] = normal_part
        rhs_ref[...] = rhs_part

    @pl.when(step > 0)
    def _():
        normal_ref[...] += normal_part
        rhs_ref[...] += rhs_part

    @pl.when(step == pl.num_programs(0) - 1)
    def _():
        normal_ref[...] = normal_ref[...] / scale
        rhs_ref[...] = rhs_ref[...] / scale


def normal_block(states, targets, block, blocks, lanes=2048):
    rank, snaps = states.shape
    width = rank + rank * (rank + 1) // 2
    count = width // blocks
    kernel = functools.partial(normal_kernel, block * count, count, float(snaps))
    return pl.pallas_call(
        kernel,
        grid=(snaps // lanes,),
        in_specs=[
            pl.BlockSpec((rank, lanes), lambda j: (0, j)),
            pl.BlockSpec((rank, lanes), lambda j: (0, j)),
        ],
        out_specs=[
            pl.BlockSpec((count, width), lambda j: (0, 0)),
            pl.BlockSpec((rank, count), lambda j: (0, 0)),
        ],
        out_shape=[
            jax.ShapeDtypeStruct((count, width), jnp.float32),
            jax.ShapeDtypeStruct((rank, count), jnp.float32),
        ],
        scratch_shapes=[pltpu.VMEM((width, lanes), jnp.float32)],
        compiler_params=pltpu.CompilerParams(vmem_limit_bytes=48 * 1024 * 1024),
        cost_estimate=pl.CostEstimate(
            flops=2 * count * (width + rank) * snaps,
            transcendentals=0,
            bytes_accessed=rank * snaps * 6 + count * (width + rank) * 4,
        ),
    )(states, targets)


def per_device(snapshots, basis):
    partial_value = lax.dot_general(
        basis, snapshots, (((0,), (0,)), ((), ())), preferred_element_type=jnp.float32
    )
    rank, columns = partial_value.shape
    chips = lax.axis_size("chip")
    cores = lax.axis_size("core")
    snaps = lax.axis_size("snap")
    pair = partial_value.reshape(cores, chips, columns).transpose(1, 0, 2)
    send = jnp.broadcast_to(pair[:, None], (chips, cores, cores, columns)).reshape(rank, cores, columns)
    received = lax.all_to_all(send, ("chip", "core"), 0, 0, tiled=True)
    owned = jnp.sum(received, axis=0, keepdims=True)
    spread = jnp.broadcast_to(owned, (chips * snaps, cores, columns))
    rows = lax.all_to_all(spread, ("chip", "snap"), 0, 0, tiled=True)
    states = rows.reshape(chips, snaps, cores, columns).transpose(2, 0, 1, 3).reshape(rank, snaps * columns)
    targets = (jnp.roll(states, -1, axis=1) - states).astype(jnp.bfloat16)
    branches = [functools.partial(normal_block, block=b, blocks=snaps) for b in range(snaps)]
    normal, rhs_t = lax.switch(lax.axis_index("snap"), branches, states, targets)
    return (normal, rhs_t.T)


def solution(mesh):
    space, snaps = mesh.devices.shape
    chip_mesh = jax.sharding.Mesh(
        mesh.devices.reshape(space // 2, 2, snaps), ("chip", "core", mesh.axis_names[1])
    )
    return jax.shard_map(
        per_device,
        mesh=chip_mesh,
        in_specs=(P(("chip", "core"), "snap"), P(("chip", "core"), None)),
        out_specs=(P("snap", None), P("snap", None)),
        check_vma=False,
    )
```

```python
import functools

import jax
import jax.numpy as jnp
import numpy as np
from jax import lax
from jax.experimental import pallas as pl
from jax.experimental.pallas import tpu as pltpu
from jax.sharding import PartitionSpec as P


def swapped(block, axis, distance):
    count = lax.axis_size(axis)
    return lax.ppermute(block, axis, [(i, i ^ distance) for i in range(count)])


def butterfly_sum(block, axis):
    distance = 1
    while distance < lax.axis_size(axis):
        block = block + swapped(block, axis, distance)
        distance *= 2
    return block


def butterfly_gather(block, axis):
    index = lax.axis_index(axis)
    distance = 1
    while distance < lax.axis_size(axis):
        other = swapped(block, axis, distance)
        low = (index // distance) % 2 == 0
        block = jnp.where(
            low,
            jnp.concatenate([block, other], axis=1),
            jnp.concatenate([other, block], axis=1),
        )
        distance *= 2
    return block


def fill_rows(states_ref, rows_ref):
    rank = states_ref.shape[0]
    rows_ref[0:rank, :] = states_ref[...]
    offset = rank
    for a in range(rank):
        count = rank - a
        rows_ref[offset : offset + count, :] = states_ref[a : a + 1, :] * states_ref[a:rank, :]
        offset += count


def normal_kernel(first, count, scale, states_ref, normal_ref, rhs_ref, rows_ref):
    step = pl.program_id(0)
    fill_rows(states_ref, rows_ref)
    feats = rows_ref[...].astype(jnp.bfloat16)
    chosen = rows_ref[first : first + count, :].astype(jnp.bfloat16)
    dims = (((1,), (1,)), ((), ()))
    normal_part = lax.dot_general(chosen, feats, dims, preferred_element_type=jnp.float32)
    snaps = states_ref.shape[1]
    following = pltpu.roll(states_ref[...], snaps - 1, 1)
    targets = (following - states_ref[...]).astype(jnp.bfloat16)
    rhs_part = lax.dot_general(targets, chosen, dims, preferred_element_type=jnp.float32)

    @pl.when(step == 0)
    def _():
        normal_ref[...] = normal_part
        rhs_ref[...] = rhs_part

    @pl.when(step > 0)
    def _():
        normal_ref[...] += normal_part
        rhs_ref[...] += rhs_part

    @pl.when(step == pl.num_programs(0) - 1)
    def _():
        normal_ref[...] = normal_ref[...] / scale
        rhs_ref[...] = rhs_ref[...] / scale


def normal_block(states, block, blocks, lanes=2048):
    rank, snaps = states.shape
    width = rank + rank * (rank + 1) // 2
    count = width // blocks
    kernel = functools.partial(normal_kernel, block * count, count, float(snaps))
    return pl.pallas_call(
        kernel,
        grid=(snaps // lanes,),
        in_specs=[pl.BlockSpec((rank, lanes), lambda j: (0, j))],
        out_specs=[
            pl.BlockSpec((count, width), lambda j: (0, 0)),
            pl.BlockSpec((rank, count), lambda j: (0, 0)),
        ],
        out_shape=[
            jax.ShapeDtypeStruct((count, width), jnp.float32),
            jax.ShapeDtypeStruct((rank, count), jnp.float32),
        ],
        scratch_shapes=[pltpu.VMEM((width, lanes), jnp.float32)],
        compiler_params=pltpu.CompilerParams(vmem_limit_bytes=48 * 1024 * 1024),
        cost_estimate=pl.CostEstimate(
            flops=2 * count * (width + rank) * snaps,
            transcendentals=0,
            bytes_accessed=rank * snaps * 6 + count * (width + rank) * 4,
        ),
    )(states)


def per_device(snapshots, basis):
    partial_value = lax.dot_general(
        basis, snapshots, (((0,), (0,)), ((), ())), preferred_element_type=jnp.float32
    )
    rank, columns = partial_value.shape
    chips = lax.axis_size("chip")
    cores = lax.axis_size("core")
    snaps = lax.axis_size("snap")
    core = lax.axis_index("core")
    by_chip = partial_value.reshape(cores, chips, columns).transpose(1, 0, 2).reshape(rank, columns)
    received = lax.all_to_all(by_chip, ("chip", "core"), 0, 0, tiled=True)
    owned = jnp.sum(received, axis=0, keepdims=True)
    spread = jnp.broadcast_to(owned, (chips * snaps, columns))
    half = lax.all_to_all(spread, ("chip", "snap"), 0, 0, tiled=True).reshape(chips, snaps * columns)
    other = lax.ppermute(half, "core", [(0, 1), (1, 0)])
    states = jnp.where(
        core == 0,
        jnp.concatenate([half, other], axis=0),
        jnp.concatenate([other, half], axis=0),
    )
    branches = [functools.partial(normal_block, block=b, blocks=snaps) for b in range(snaps)]
    normal, rhs_t = lax.switch(lax.axis_index("snap"), branches, states)
    return (normal, rhs_t.T)


def solution(mesh):
    space, snaps = mesh.devices.shape
    chip_mesh = jax.sharding.Mesh(
        mesh.devices.reshape(space // 2, 2, snaps), ("chip", "core", mesh.axis_names[1])
    )
    return jax.shard_map(
        per_device,
        mesh=chip_mesh,
        in_specs=(P(("chip", "core"), "snap"), P(("chip", "core"), None)),
        out_specs=(P("snap", None), P("snap", None)),
        check_vma=False,
    )
```
